1024 devices in a mesh: dp: 128 (over z, x_hi, core), tp: 8 (over y, x_lo).
Axes of the slice: x: 4 (x_hi: 2, x_lo: 2; x = x_hi * 2 + x_lo), y: 4, z: 32, core: 2. Of those that a mesh axis runs over, the one named last changes fastest.
Arguments:
- hidden: bfloat16 [4, 6144, 8192], P(None, 'dp'), may hold values from -6 to 6
- kv_weight: bfloat16 [8192, 2048], P(('dp', 'tp')), may hold values from -0.0625 to 0.0625
- queries: bfloat16 [4, 6144, 8192], P(None, 'dp', 'tp'), may hold values from -6 to 6
- kv_cache: bfloat16 [6144, 8, 2, 96, 128], P('dp', 'tp'), may hold values from -6 to 6
- lengths: int32 [6144], P('dp'), may hold values from 2 to 92, as said below
- out_gain: bfloat16 [8192], replicated, may hold values from 0.5 to 1.5
Outputs:
- returned: bfloat16 [4, 6144, 8192], P(None, ('dp', 'tp'))
The draws below stay inside these ranges and needn't reach their ends.
Inputs may be any that keep to these rules, and one draw needn't show every extreme that they name: `lengths`: some row has exactly 92 valid positions.
All inputs are finite; a program needn't handle non-finite values.
Results may differ from the reference program's by a relative error of at most 0.0085.
Values may be sent and summed in bfloat16 or wider, within the bound.
No kernel may reach another device: no remote copies, remote signals or barrier semaphores. Data moves between devices by JAX's collectives and lax.ppermute only.
A program may use at most 32 MiB of HBM per device.

```python
import jax
import jax.numpy as jnp
from jax import lax

D = 8192
H = 64
KVH = 8
HD = 128
STEPS = 4
CACHE = 96
ROWS = 6144


def draw_lengths(key, part):
    first, second = jax.random.split(key)
    picked = jax.random.randint(first, (ROWS,), 2, CACHE - STEPS + 1)
    where_most = jax.random.randint(second, (), 0, ROWS)
    return picked.at[where_most].set(CACHE - STEPS).astype(jnp.int32)


def aligned_pattern(key):
    shared = jax.random.fold_in(key, 7)
    first, second = jax.random.split(shared)
    signs = jnp.where(jax.random.bernoulli(first, 0.5, (ROWS, KVH, HD)), 1.0, -1.0).astype(jnp.float32)
    offset = jax.random.randint(second, (), 0, 8)
    row_ids = jnp.arange(ROWS)
    chosen = row_ids % 8 == offset
    level = row_ids // 8 % 3
    strength = jnp.where(level == 0, 3.75, jnp.where(level == 1, 4.75, 6.0)).astype(jnp.float32)
    return (signs, chosen, strength)


def base_values(key, shape):
    return jnp.clip(jax.random.normal(key, shape, jnp.float32), -6.0, 6.0)


def draw_queries(key, part):
    signs, chosen, strength = aligned_pattern(key)
    base = base_values(jax.random.fold_in(key, 11), (STEPS, ROWS, H * HD))
    per_group = H // KVH
    pattern = strength[:, None, None] * signs
    pattern = jnp.broadcast_to(pattern[:, :, None, :], (ROWS, KVH, per_group, HD)).reshape(ROWS, H * HD)
    picked = jnp.where(chosen[None, :, None], pattern[None, :, :], base)
    return picked.astype(jnp.bfloat16)


def draw_kv_cache(key, part):
    signs, chosen, strength = aligned_pattern(key)
    base = base_values(jax.random.fold_in(key, 13), (ROWS, KVH, 2, CACHE, HD))
    first_key = strength[:, None, None] * signs
    lowered = 2.0 * jnp.sqrt(jnp.float32(HD)) / strength
    second_key = first_key.at[:, :, 0].add(-signs[:, :, 0] * lowered[:, None])
    positions = jnp.arange(CACHE)[None, None, :, None]
    aligned = jnp.where(positions == 0, first_key[:, :, None, :], second_key[:, :, None, :])
    mask = chosen[:, None, None, None] & (positions < 2)
    keys_part = jnp.where(mask, aligned, base[:, :, 0])
    stacked = jnp.stack([keys_part, base[:, :, 1]], axis=2)
    return stacked.astype(jnp.bfloat16)


def shard_levels(rng, dims, pieces, least, high):
    loudness, own = 1.0, jax.random.fold_in(rng, 6)
    for dim, parts in pieces:
        heights = jnp.exp(jax.random.uniform(jax.random.fold_in(own, dim), (parts,), jnp.float32, least / len(pieces), high / len(pieces)))
        loudness = loudness * jnp.repeat(heights, dims[dim] // parts).reshape([-1 if axis == dim else 1 for axis in range(len(dims))])
    return loudness


def bell_draw(own_key, shape, spread, bound, cuts=(), kind=jnp.bfloat16):
    factor_of = shard_levels(own_key, shape, cuts, -0.22, 0.18) if cuts else 1.0
    entries = jax.random.normal(own_key, shape, jnp.float32) * spread * factor_of
    return jnp.minimum(jnp.maximum(entries, -bound), bound).astype(kind)


def setup_inputs(seed: int = 0) -> dict:
    splits = jax.random.split(jax.random.key(seed), 7)
    hidden = bell_draw(splits[0], (STEPS, ROWS, D), 1.0, 6.0, ((1, 128),))
    kv_weight = bell_draw(splits[1], (D, KVH * 2 * HD), D ** -0.5, 0.0625, ((0, 1024),))
    queries = draw_queries(jax.random.fold_in(splits[6], 71), 0)
    kv_cache = draw_kv_cache(jax.random.fold_in(splits[6], 71), 0)
    lengths = draw_lengths(jax.random.fold_in(splits[6], 71), 0)
    out_gain = jnp.clip(1.0 + 0.1 * jax.random.normal(splits[5], (H * HD,), jnp.float32), 0.5, 1.5).astype(jnp.bfloat16)
    return {"hidden": hidden, "kv_weight": kv_weight, "queries": queries, "kv_cache": kv_cache, "lengths": lengths, "out_gain": out_gain}


def reference(hidden, kv_weight, queries, kv_cache, lengths, out_gain):
    fresh = jnp.dot(hidden.reshape(STEPS * ROWS, D), kv_weight, preferred_element_type=jnp.float32)
    fresh = fresh.astype(jnp.bfloat16).reshape(STEPS, ROWS, KVH, 2, HD)
    group = H // KVH
    grouped = queries.reshape(STEPS, ROWS, KVH, group, HD)
    scale = 1.0 / jnp.sqrt(jnp.float32(HD))
    valid = jnp.arange(CACHE)[None, :] < lengths[:, None]
    causal = jnp.arange(STEPS)[:, None] >= jnp.arange(STEPS)[None, :]

    def one_group(index):
        query = lax.dynamic_index_in_dim(grouped, index, 2, False).astype(jnp.float32)
        cached = lax.dynamic_index_in_dim(kv_cache, index, 1, False).astype(jnp.float32)
        newer = lax.dynamic_index_in_dim(fresh, index, 2, False).astype(jnp.float32)
        old_scores = jnp.einsum('srpe,rce->srpc', query, cached[:, 0]) * scale
        old_scores = jnp.where(valid[None, :, None, :], old_scores, -1e+30)
        new_scores = jnp.einsum('srpe,tre->srpt', query, newer[:, :, 0]) * scale
        new_scores = jnp.where(causal[:, None, None, :], new_scores, -1e+30)
        top = jnp.maximum(lax.optimization_barrier(jnp.max(old_scores, -1, keepdims=True)), lax.optimization_barrier(jnp.max(new_scores, -1, keepdims=True)))
        old_exp = jnp.exp(old_scores - top)
        new_exp = jnp.exp(new_scores - top)
        total = lax.optimization_barrier(jnp.sum(old_exp, -1, keepdims=True)) + lax.optimization_barrier(jnp.sum(new_exp, -1, keepdims=True))
        old_weights = lax.optimization_barrier((old_exp / total).astype(jnp.bfloat16)).astype(jnp.float32)
        new_weights = lax.optimization_barrier((new_exp / total).astype(jnp.bfloat16)).astype(jnp.float32)
        mixed = jnp.einsum('srpc,rce->srpe', old_weights, cached[:, 1])
        mixed = mixed + jnp.einsum('srpt,tre->srpe', new_weights, newer[:, :, 1])
        return mixed.astype(jnp.bfloat16)
    blocks = lax.map(one_group, jnp.arange(KVH))
    attn = jnp.transpose(blocks, (1, 2, 0, 3, 4)).reshape(STEPS, ROWS, H * HD)
    values = attn.astype(jnp.float32)
    square_mean = lax.optimization_barrier(jnp.mean(values * values, -1, keepdims=True))
    normed = values * lax.rsqrt(square_mean + 1e-05) * out_gain.astype(jnp.float32)
    return normed.astype(jnp.bfloat16)
```

```python
import jax
import jax.numpy as jnp
from jax import lax
from jax.sharding import Mesh
from jax.sharding import PartitionSpec as P

DP = ("dp_0", "dp_1", "dp_2")
DP_TP = ("dp_0", "dp_1", "dp_2", "tp")


def in_order(tiles, dim):
    shape = list(tiles.shape[1:])
    shape[dim] *= tiles.shape[0]
    return jnp.moveaxis(tiles, 0, dim).reshape(shape)


def all_blocks(value, axes, sequence):
    tiles = value
    for k in sequence:
        tiles = lax.all_gather(tiles, axes[k])
    done = sequence[::-1]
    back = [done.index(k) for k in range(len(axes))]
    tiles = tiles.transpose(*back, *range(len(axes), tiles.ndim))
    return tiles.reshape(-1, *value.shape)


def gathered_by_axis(value, axes, sequence, dim):
    return in_order(all_blocks(value, axes, sequence), dim)


def per_device(hidden, kv_weight, queries, kv_cache, lengths, out_gain):
    steps, rows, width = hidden.shape
    local_groups = kv_cache.shape[1]
    own_piece = lax.all_to_all(kv_weight, "tp", split_axis=1, concat_axis=0, tiled=True)
    flat_rows = hidden.reshape(steps * rows, width)
    projected = jnp.dot(
        flat_rows, gathered_by_axis(own_piece, DP, (2, 1, 0), 0), preferred_element_type=jnp.float32
    )
    head_size = kv_cache.shape[4]
    fresh = projected.astype(jnp.bfloat16).reshape(steps, rows, local_groups, 2, head_size)
    per_group = queries.shape[2] // (local_groups * head_size)
    query = queries.reshape(steps, rows, local_groups, per_group, head_size)
    scale = 1.0 / jnp.sqrt(jnp.float32(head_size))
    cache_len = kv_cache.shape[3]
    valid = jnp.arange(cache_len)[None, :] < lengths[:, None]
    causal = jnp.arange(steps)[:, None] >= jnp.arange(steps)[None, :]
    old_scores = (
        jnp.einsum(
            "srgpe,rgce->srgpc", query, kv_cache[:, :, 0], preferred_element_type=jnp.float32
        )
        * scale
    )
    old_scores = jnp.where(valid[None, :, None, None, :], old_scores, -1e30)
    new_scores = (
        jnp.einsum(
            "srgpe,trge->srgpt", query, fresh[:, :, :, 0], preferred_element_type=jnp.float32
        )
        * scale
    )
    new_scores = jnp.where(causal[:, None, None, None, :], new_scores, -1e30)
    top = jnp.maximum(
        jnp.max(old_scores, -1, keepdims=True), jnp.max(new_scores, -1, keepdims=True)
    )
    old_exp = jnp.exp(old_scores - top)
    new_exp = jnp.exp(new_scores - top)
    total = jnp.sum(old_exp, -1, keepdims=True) + jnp.sum(new_exp, -1, keepdims=True)
    old_weights = (old_exp / total).astype(jnp.bfloat16)
    new_weights = (new_exp / total).astype(jnp.bfloat16)
    mixed = jnp.einsum(
        "srgpc,rgce->srgpe", old_weights, kv_cache[:, :, 1], preferred_element_type=jnp.float32
    )
    mixed = mixed + jnp.einsum(
        "srgpt,trge->srgpe", new_weights, fresh[:, :, :, 1], preferred_element_type=jnp.float32
    )
    attn = mixed.astype(jnp.bfloat16).reshape(steps, rows, local_groups * per_group * head_size)
    arrived = lax.all_to_all(attn, "tp", split_axis=1, concat_axis=2, tiled=True)
    values = arrived.astype(jnp.float32)
    square_mean = jnp.mean(values * values, -1, keepdims=True)
    normed = values * lax.rsqrt(square_mean + 1e-05) * out_gain.astype(jnp.float32)
    return normed.astype(jnp.bfloat16)


def solution(mesh):
    torus = Mesh(mesh.devices.reshape(32, 2, 2, mesh.shape["tp"]), ("dp_0", "dp_1", "dp_2", "tp"))
    return jax.shard_map(
        per_device,
        mesh=torus,
        in_specs=(
            P(None, DP, None),
            P(DP_TP, None),
            P(None, DP, "tp"),
            P(DP, "tp", None, None, None),
            P(DP),
            P(),
        ),
        out_specs=P(None, DP_TP, None),
        check_vma=False,
    )
```

```python
import jax
import jax.numpy as jnp
from jax import lax
from jax.sharding import Mesh
from jax.sharding import PartitionSpec as P

DP = ("dp_0a", "dp_0b", "dp_1", "dp_2")
DP_TP = ("dp_0a", "dp_0b", "dp_1", "dp_2", "tp")


def in_order(tiles, dim):
    shape = list(tiles.shape[1:])
    shape[dim] *= tiles.shape[0]
    return jnp.moveaxis(tiles, 0, dim).reshape(shape)


def all_blocks(value, axes, sequence):
    tiles = value
    for k in sequence:
        tiles = lax.all_gather(tiles, axes[k])
    done = sequence[::-1]
    back = [done.index(k) for k in range(len(axes))]
    tiles = tiles.transpose(*back, *range(len(axes), tiles.ndim))
    return tiles.reshape(-1, *value.shape)


def gathered_by_axis(value, axes, sequence, dim):
    return in_order(all_blocks(value, axes, sequence), dim)


def pp_gather(x, axis, n):
    me = lax.axis_index(axis)
    pieces = [x] + [lax.ppermute(x, axis, [(k, (k + d) % n) for k in range(n)]) for d in range(1, n)]
    rel = jnp.stack(pieces)
    return jnp.take(rel, (me - jnp.arange(n)) % n, axis=0)


def gather_w(own_piece, zb_pp, core_pp):
    t = lax.all_gather(own_piece, "dp_1")
    t = lax.all_gather(t, "dp_0a")
    t = pp_gather(t, "dp_0b", 4) if zb_pp else lax.all_gather(t, "dp_0b")
    t = pp_gather(t, "dp_2", 2) if core_pp else lax.all_gather(t, "dp_2")
    return t.transpose(2, 1, 3, 0, 4, 5).reshape(-1, own_piece.shape[1])


def per_device(hidden, kv_weight, queries, kv_cache, lengths, out_gain):
    steps, rows, width = hidden.shape
    local_groups = kv_cache.shape[1]
    own_piece = lax.all_to_all(kv_weight, "tp", split_axis=1, concat_axis=0, tiled=True)
    flat_rows = hidden.reshape(steps * rows, width)
    projected = jnp.dot(
        flat_rows, gather_w(own_piece, True, True), preferred_element_type=jnp.float32
    )
    head_size = kv_cache.shape[4]
    fresh = projected.astype(jnp.bfloat16).reshape(steps, rows, local_groups, 2, head_size)
    per_group = queries.shape[2] // (local_groups * head_size)
    query = queries.reshape(steps, rows, local_groups, per_group, head_size)
    scale = 1.0 / jnp.sqrt(jnp.float32(head_size))
    cache_len = kv_cache.shape[3]
    valid = jnp.arange(cache_len)[None, :] < lengths[:, None]
    causal = jnp.arange(steps)[:, None] >= jnp.arange(steps)[None, :]
    old_scores = (
        jnp.einsum(
            "srgpe,rgce->srgpc", query, kv_cache[:, :, 0], preferred_element_type=jnp.float32
        )
        * scale
    )
    old_scores = jnp.where(valid[None, :, None, None, :], old_scores, -1e30)
    new_scores = (
        jnp.einsum(
            "srgpe,trge->srgpt", query, fresh[:, :, :, 0], preferred_element_type=jnp.float32
        )
        * scale
    )
    new_scores = jnp.where(causal[:, None, None, None, :], new_scores, -1e30)
    top = jnp.maximum(
        jnp.max(old_scores, -1, keepdims=True), jnp.max(new_scores, -1, keepdims=True)
    )
    old_exp = jnp.exp(old_scores - top)
    new_exp = jnp.exp(new_scores - top)
    total = jnp.sum(old_exp, -1, keepdims=True) + jnp.sum(new_exp, -1, keepdims=True)
    old_weights = (old_exp / total).astype(jnp.bfloat16)
    new_weights = (new_exp / total).astype(jnp.bfloat16)
    mixed = jnp.einsum(
        "srgpc,rgce->srgpe", old_weights, kv_cache[:, :, 1], preferred_element_type=jnp.float32
    )
    mixed = mixed + jnp.einsum(
        "srgpt,trge->srgpe", new_weights, fresh[:, :, :, 1], preferred_element_type=jnp.float32
    )
    attn = mixed.astype(jnp.bfloat16).reshape(steps, rows, local_groups * per_group * head_size)
    arrived = lax.all_to_all(attn, "tp", split_axis=1, concat_axis=2, tiled=True)
    values = arrived.astype(jnp.float32)
    square_mean = jnp.mean(values * values, -1, keepdims=True)
    normed = values * lax.rsqrt(square_mean + 1e-05) * out_gain.astype(jnp.float32)
    return normed.astype(jnp.bfloat16)


def solution(mesh):
    torus = Mesh(mesh.devices.reshape(8, 4, 2, 2, mesh.shape["tp"]), ("dp_0a", "dp_0b", "dp_1", "dp_2", "tp"))
    return jax.shard_map(
        per_device,
        mesh=torus,
        in_specs=(
            P(None, DP, None),
            P(DP_TP, None),
            P(None, DP, "tp"),
            P(DP, "tp", None, None, None),
            P(DP),
            P(),
        ),
        out_specs=P(None, DP_TP, None),
        check_vma=False,
    )
```

```python
import jax
import jax.numpy as jnp
from jax import lax
from jax.sharding import Mesh
from jax.sharding import PartitionSpec as P

DP = ("dp_0a", "dp_0b", "dp_1", "dp_2")
DP_TP = ("dp_0a", "dp_0b", "dp_1", "dp_2", "tp")


def in_order(tiles, dim):
    shape = list(tiles.shape[1:])
    shape[dim] *= tiles.shape[0]
    return jnp.moveaxis(tiles, 0, dim).reshape(shape)


def all_blocks(value, axes, sequence):
    tiles = value
    for k in sequence:
        tiles = lax.all_gather(tiles, axes[k])
    done = sequence[::-1]
    back = [done.index(k) for k in range(len(axes))]
    tiles = tiles.transpose(*back, *range(len(axes), tiles.ndim))
    return tiles.reshape(-1, *value.shape)


def gathered_by_axis(value, axes, sequence, dim):
    return in_order(all_blocks(value, axes, sequence), dim)


def pp_gather(x, axis, n):
    spread = jnp.broadcast_to(x[None], (n,) + x.shape)
    return lax.all_to_all(spread, axis, 0, 0, tiled=True)


def gather_w(own_piece, zb_pp, core_pp):
    t = lax.all_gather(own_piece, "dp_1")
    t = lax.all_gather(t, "dp_0a")
    t = pp_gather(t, "dp_0b", 4) if zb_pp else lax.all_gather(t, "dp_0b")
    t = pp_gather(t, "dp_2", 2) if core_pp else lax.all_gather(t, "dp_2")
    return t.transpose(2, 1, 3, 0, 4, 5).reshape(-1, own_piece.shape[1])


def per_device(hidden, kv_weight, queries, kv_cache, lengths, out_gain):
    steps, rows, width = hidden.shape
    local_groups = kv_cache.shape[1]
    own_piece = lax.all_to_all(kv_weight, "tp", split_axis=1, concat_axis=0, tiled=True)
    flat_rows = hidden.reshape(steps * rows, width)
    projected = jnp.dot(
        flat_rows, gather_w(own_piece, True, True), preferred_element_type=jnp.float32
    )
    head_size = kv_cache.shape[4]
    fresh = projected.astype(jnp.bfloat16).reshape(steps, rows, local_groups, 2, head_size)
    per_group = queries.shape[2] // (local_groups * head_size)
    query = queries.reshape(steps, rows, local_groups, per_group, head_size)
    scale = 1.0 / jnp.sqrt(jnp.float32(head_size))
    cache_len = kv_cache.shape[3]
    valid = jnp.arange(cache_len)[None, :] < lengths[:, None]
    causal = jnp.arange(steps)[:, None] >= jnp.arange(steps)[None, :]
    old_scores = (
        jnp.einsum(
            "srgpe,rgce->srgpc", query, kv_cache[:, :, 0], preferred_element_type=jnp.float32
        )
        * scale
    )
    old_scores = jnp.where(valid[None, :, None, None, :], old_scores, -1e30)
    new_scores = (
        jnp.einsum(
            "srgpe,trge->srgpt", query, fresh[:, :, :, 0], preferred_element_type=jnp.float32
        )
        * scale
    )
    new_scores = jnp.where(causal[:, None, None, None, :], new_scores, -1e30)
    top = jnp.maximum(
        jnp.max(old_scores, -1, keepdims=True), jnp.max(new_scores, -1, keepdims=True)
    )
    old_exp = jnp.exp(old_scores - top)
    new_exp = jnp.exp(new_scores - top)
    total = jnp.sum(old_exp, -1, keepdims=True) + jnp.sum(new_exp, -1, keepdims=True)
    old_weights = (old_exp / total).astype(jnp.bfloat16)
    new_weights = (new_exp / total).astype(jnp.bfloat16)
    mixed = jnp.einsum(
        "srgpc,rgce->srgpe", old_weights, kv_cache[:, :, 1], preferred_element_type=jnp.float32
    )
    mixed = mixed + jnp.einsum(
        "srgpt,trge->srgpe", new_weights, fresh[:, :, :, 1], preferred_element_type=jnp.float32
    )
    attn = mixed.astype(jnp.bfloat16).reshape(steps, rows, local_groups * per_group * head_size)
    arrived = lax.all_to_all(attn, "tp", split_axis=1, concat_axis=2, tiled=True)
    values = arrived.astype(jnp.float32)
    square_mean = jnp.mean(values * values, -1, keepdims=True)
    normed = values * lax.rsqrt(square_mean + 1e-05) * out_gain.astype(jnp.float32)
    return normed.astype(jnp.bfloat16)


def solution(mesh):
    torus = Mesh(mesh.devices.reshape(8, 4, 2, 2, mesh.shape["tp"]), ("dp_0a", "dp_0b", "dp_1", "dp_2", "tp"))
    return jax.shard_map(
        per_device,
        mesh=torus,
        in_specs=(
            P(None, DP, None),
            P(DP_TP, None),
            P(None, DP, "tp"),
            P(DP, "tp", None, None, None),
            P(DP),
            P(),
        ),
        out_specs=P(None, DP_TP, None),
        check_vma=False,
    )
```

```python
import jax
import jax.numpy as jnp
from jax import lax
from jax.sharding import Mesh
from jax.sharding import PartitionSpec as P

DP = ("dp_0a", "dp_0b", "dp_1", "dp_2")
DP_TP = ("dp_0a", "dp_0b", "dp_1", "dp_2", "tp")


def in_order(tiles, dim):
    shape = list(tiles.shape[1:])
    shape[dim] *= tiles.shape[0]
    return jnp.moveaxis(tiles, 0, dim).reshape(shape)


def all_blocks(value, axes, sequence):
    tiles = value
    for k in sequence:
        tiles = lax.all_gather(tiles, axes[k])
    done = sequence[::-1]
    back = [done.index(k) for k in range(len(axes))]
    tiles = tiles.transpose(*back, *range(len(axes), tiles.ndim))
    return tiles.reshape(-1, *value.shape)


def gathered_by_axis(value, axes, sequence, dim):
    return in_order(all_blocks(value, axes, sequence), dim)


def pp_gather(x, axis, n):
    spread = jnp.broadcast_to(x[None], (n,) + x.shape)
    return lax.all_to_all(spread, axis, 0, 0, tiled=True)


def gather_w(kv_weight, groups):
    rows, width = kv_weight.shape
    cols = width // groups
    mine = kv_weight.reshape(rows, groups, cols).transpose(1, 0, 2)
    spread = jnp.broadcast_to(mine[None], (2,) + mine.shape).reshape(2 * groups, rows, cols)
    t = lax.all_to_all(spread, ("dp_1", "tp"), 0, 0, tiled=True).reshape(2, groups, rows, cols)
    t = lax.all_gather(t, "dp_0a")
    t = pp_gather(t, "dp_0b", 4)
    t = pp_gather(t, "dp_2", 2)
    return t.transpose(2, 1, 3, 0, 4, 5, 6).reshape(-1, cols)

def per_device(hidden, kv_weight, queries, kv_cache, lengths, out_gain):
    steps, rows, width = hidden.shape
    local_groups = kv_cache.shape[1]
    flat_rows = hidden.reshape(steps * rows, width)
    projected = jnp.dot(
        flat_rows, gather_w(kv_weight, kv_weight.shape[1] // (2 * kv_cache.shape[4])), preferred_element_type=jnp.float32
    )
    head_size = kv_cache.shape[4]
    fresh = projected.astype(jnp.bfloat16).reshape(steps, rows, local_groups, 2, head_size)
    per_group = queries.shape[2] // (local_groups * head_size)
    query = queries.reshape(steps, rows, local_groups, per_group, head_size)
    scale = 1.0 / jnp.sqrt(jnp.float32(head_size))
    cache_len = kv_cache.shape[3]
    valid = jnp.arange(cache_len)[None, :] < lengths[:, None]
    causal = jnp.arange(steps)[:, None] >= jnp.arange(steps)[None, :]
    old_scores = (
        jnp.einsum(
            "srgpe,rgce->srgpc", query, kv_cache[:, :, 0], preferred_element_type=jnp.float32
        )
        * scale
    )
    old_scores = jnp.where(valid[None, :, None, None, :], old_scores, -1e30)
    new_scores = (
        jnp.einsum(
            "srgpe,trge->srgpt", query, fresh[:, :, :, 0], preferred_element_type=jnp.float32
        )
        * scale
    )
    new_scores = jnp.where(causal[:, None, None, None, :], new_scores, -1e30)
    top = jnp.maximum(
        jnp.max(old_scores, -1, keepdims=True), jnp.max(new_scores, -1, keepdims=True)
    )
    old_exp = jnp.exp(old_scores - top)
    new_exp = jnp.exp(new_scores - top)
    total = jnp.sum(old_exp, -1, keepdims=True) + jnp.sum(new_exp, -1, keepdims=True)
    old_weights = (old_exp / total).astype(jnp.bfloat16)
    new_weights = (new_exp / total).astype(jnp.bfloat16)
    mixed = jnp.einsum(
        "srgpc,rgce->srgpe", old_weights, kv_cache[:, :, 1], preferred_element_type=jnp.float32
    )
    mixed = mixed + jnp.einsum(
        "srgpt,trge->srgpe", new_weights, fresh[:, :, :, 1], preferred_element_type=jnp.float32
    )
    attn = mixed.astype(jnp.bfloat16).reshape(steps, rows, local_groups * per_group * head_size)
    arrived = lax.all_to_all(attn, "tp", split_axis=1, concat_axis=2, tiled=True)
    values = arrived.astype(jnp.float32)
    square_mean = jnp.mean(values * values, -1, keepdims=True)
    normed = values * lax.rsqrt(square_mean + 1e-05) * out_gain.astype(jnp.float32)
    return normed.astype(jnp.bfloat16)


def solution(mesh):
    torus = Mesh(mesh.devices.reshape(8, 4, 2, 2, mesh.shape["tp"]), ("dp_0a", "dp_0b", "dp_1", "dp_2", "tp"))
    return jax.shard_map(
        per_device,
        mesh=torus,
        in_specs=(
            P(None, DP, None),
            P(DP_TP, None),
            P(None, DP, "tp"),
            P(DP, "tp", None, None, None),
            P(DP),
            P(),
        ),
        out_specs=P(None, DP_TP, None),
        check_vma=False,
    )
```

```python
import jax
import jax.numpy as jnp
from jax import lax
from jax.sharding import Mesh
from jax.sharding import PartitionSpec as P

DP = ("dp_0a", "dp_0b", "dp_1", "dp_2")
DP_TP = ("dp_0a", "dp_0b", "dp_1", "dp_2", "tp")


def in_order(tiles, dim):
    shape = list(tiles.shape[1:])
    shape[dim] *= tiles.shape[0]
    return jnp.moveaxis(tiles, 0, dim).reshape(shape)


def all_blocks(value, axes, sequence):
    tiles = value
    for k in sequence:
        tiles = lax.all_gather(tiles, axes[k])
    done = sequence[::-1]
    back = [done.index(k) for k in range(len(axes))]
    tiles = tiles.transpose(*back, *range(len(axes), tiles.ndim))
    return tiles.reshape(-1, *value.shape)


def gathered_by_axis(value, axes, sequence, dim):
    return in_order(all_blocks(value, axes, sequence), dim)


def pp_gather(x, axis, n):
    spread = jnp.broadcast_to(x[None], (n,) + x.shape)
    return lax.all_to_all(spread, axis, 0, 0, tiled=True)


def gather_w(kv_weight, groups):
    rows, width = kv_weight.shape
    cols = width // groups
    mine = kv_weight.reshape(rows, groups, cols).transpose(1, 0, 2)
    spread = jnp.broadcast_to(mine[None], (2,) + mine.shape).reshape(2 * groups, rows, cols)
    t = lax.all_to_all(spread, ("dp_1", "tp"), 0, 0, tiled=True).reshape(2, groups, rows, cols)
    t = lax.all_gather(t, "dp_0a")
    t = pp_gather(t, "dp_0b", 4)
    t = pp_gather(t, "dp_2", 2)
    return t.transpose(2, 1, 3, 0, 4, 5, 6).reshape(-1, cols)

def per_device(hidden, kv_weight, queries, kv_cache, lengths, out_gain):
    steps, rows, width = hidden.shape
    local_groups = kv_cache.shape[1]
    flat_rows = hidden.reshape(steps * rows, width)
    projected = jnp.dot(
        flat_rows, gather_w(kv_weight, kv_weight.shape[1] // (2 * kv_cache.shape[4])), preferred_element_type=jnp.float32
    )
    head_size = kv_cache.shape[4]
    fresh = projected.astype(jnp.bfloat16).reshape(steps, rows, local_groups, 2, head_size)
    per_group = queries.shape[2] // (local_groups * head_size)
    query = queries.reshape(steps, rows, local_groups, per_group, head_size)
    scale = 1.0 / jnp.sqrt(jnp.float32(head_size))
    cache_len = kv_cache.shape[3]
    valid = jnp.arange(cache_len)[None, :] < lengths[:, None]
    causal = jnp.arange(steps)[:, None] >= jnp.arange(steps)[None, :]
    old_scores = (
        jnp.einsum(
            "srgpe,rgce->srgpc", query, kv_cache[:, :, 0], preferred_element_type=jnp.float32
        )
        * scale
    )
    old_scores = jnp.where(valid[None, :, None, None, :], old_scores, -1e30)
    new_scores = (
        jnp.einsum(
            "srgpe,trge->srgpt", query, fresh[:, :, :, 0], preferred_element_type=jnp.float32
        )
        * scale
    )
    new_scores = jnp.where(causal[:, None, None, None, :], new_scores, -1e30)
    top = jnp.maximum(
        jnp.max(old_scores, -1, keepdims=True), jnp.max(new_scores, -1, keepdims=True)
    )
    old_exp = jnp.exp(old_scores - top)
    new_exp = jnp.exp(new_scores - top)
    total = jnp.sum(old_exp, -1, keepdims=True) + jnp.sum(new_exp, -1, keepdims=True)
    old_weights = (old_exp / total).astype(jnp.bfloat16)
    new_weights = (new_exp / total).astype(jnp.bfloat16)
    mixed = jnp.einsum(
        "srgpc,rgce->srgpe", old_weights, kv_cache[:, :, 1], preferred_element_type=jnp.float32
    )
    mixed = mixed + jnp.einsum(
        "srgpt,trge->srgpe", new_weights, fresh[:, :, :, 1], preferred_element_type=jnp.float32
    )
    attn = mixed.astype(jnp.bfloat16).reshape(steps, rows, local_groups * per_group * head_size)
    parts = lax.psum(1, "tp")
    blocks = attn.reshape(steps, parts, rows // parts, attn.shape[2])
    arrived = lax.all_to_all(blocks, "tp", split_axis=1, concat_axis=1, tiled=True)
    values = arrived.astype(jnp.float32)
    square_mean = jnp.mean(values * values, (1, 3), keepdims=True)
    gain = out_gain.astype(jnp.float32).reshape(1, parts, 1, attn.shape[2])
    normed = (values * lax.rsqrt(square_mean + 1e-05) * gain).astype(jnp.bfloat16)
    return normed.transpose(0, 2, 1, 3).reshape(steps, rows // parts, parts * attn.shape[2])


def solution(mesh):
    torus = Mesh(mesh.devices.reshape(8, 4, 2, 2, mesh.shape["tp"]), ("dp_0a", "dp_0b", "dp_1", "dp_2", "tp"))
    return jax.shard_map(
        per_device,
        mesh=torus,
        in_specs=(
            P(None, DP, None),
            P(DP_TP, None),
            P(None, DP, "tp"),
            P(DP, "tp", None, None, None),
            P(DP),
            P(),
        ),
        out_specs=P(None, DP_TP, None),
        check_vma=False,
    )
```

```python
import jax
import jax.numpy as jnp
from jax import lax
from jax.sharding import Mesh
from jax.sharding import PartitionSpec as P

DP = ("dp_0a", "dp_0b", "dp_1", "dp_2")
DP_TP = ("dp_0a", "dp_0b", "dp_1", "dp_2", "tp")


def in_order(tiles, dim):
    shape = list(tiles.shape[1:])
    shape[dim] *= tiles.shape[0]
    return jnp.moveaxis(tiles, 0, dim).reshape(shape)


def all_blocks(value, axes, sequence):
    tiles = value
    for k in sequence:
        tiles = lax.all_gather(tiles, axes[k])
    done = sequence[::-1]
    back = [done.index(k) for k in range(len(axes))]
    tiles = tiles.transpose(*back, *range(len(axes), tiles.ndim))
    return tiles.reshape(-1, *value.shape)


def gathered_by_axis(value, axes, sequence, dim):
    return in_order(all_blocks(value, axes, sequence), dim)


def pp_gather(x, axis, n):
    spread = jnp.broadcast_to(x[None], (n,) + x.shape)
    return lax.all_to_all(spread, axis, 0, 0, tiled=True)


def gather_w(kv_weight, groups):
    rows, width = kv_weight.shape
    cols = width // groups
    mine = kv_weight.reshape(rows, groups, cols).transpose(1, 0, 2)
    spread = jnp.broadcast_to(mine[None], (2,) + mine.shape).reshape(2 * groups, rows, cols)
    t = lax.all_to_all(spread, ("dp_1", "tp"), 0, 0, tiled=True).reshape(2, groups, rows, cols)
    t = lax.all_gather(t, "dp_0a")
    shape = t.shape
    t = pp_gather(t.reshape(-1, cols), "dp_0b", 4)
    t = pp_gather(t.reshape(-1, cols), "dp_2", 2).reshape((2, 4) + shape)
    return t.transpose(2, 1, 3, 0, 4, 5, 6).reshape(-1, cols)

def per_device(hidden, kv_weight, queries, kv_cache, lengths, out_gain):
    steps, rows, width = hidden.shape
    local_groups = kv_cache.shape[1]
    flat_rows = hidden.reshape(steps * rows, width)
    projected = jnp.dot(
        flat_rows, gather_w(kv_weight, kv_weight.shape[1] // (2 * kv_cache.shape[4])), preferred_element_type=jnp.float32
    )
    head_size = kv_cache.shape[4]
    fresh = projected.astype(jnp.bfloat16).reshape(steps, rows, local_groups, 2, head_size)
    per_group = queries.shape[2] // (local_groups * head_size)
    query = queries.reshape(steps, rows, local_groups, per_group, head_size)
    scale = 1.0 / jnp.sqrt(jnp.float32(head_size))
    cache_len = kv_cache.shape[3]
    valid = jnp.arange(cache_len)[None, :] < lengths[:, None]
    causal = jnp.arange(steps)[:, None] >= jnp.arange(steps)[None, :]
    old_scores = (
        jnp.einsum(
            "srgpe,rgce->srgpc", query, kv_cache[:, :, 0], preferred_element_type=jnp.float32
        )
        * scale
    )
    old_scores = jnp.where(valid[None, :, None, None, :], old_scores, -1e30)
    new_scores = (
        jnp.einsum(
            "srgpe,trge->srgpt", query, fresh[:, :, :, 0], preferred_element_type=jnp.float32
        )
        * scale
    )
    new_scores = jnp.where(causal[:, None, None, None, :], new_scores, -1e30)
    top = jnp.maximum(
        jnp.max(old_scores, -1, keepdims=True), jnp.max(new_scores, -1, keepdims=True)
    )
    old_exp = jnp.exp(old_scores - top)
    new_exp = jnp.exp(new_scores - top)
    total = jnp.sum(old_exp, -1, keepdims=True) + jnp.sum(new_exp, -1, keepdims=True)
    old_weights = (old_exp / total).astype(jnp.bfloat16)
    new_weights = (new_exp / total).astype(jnp.bfloat16)
    mixed = jnp.einsum(
        "srgpc,rgce->srgpe", old_weights, kv_cache[:, :, 1], preferred_element_type=jnp.float32
    )
    mixed = mixed + jnp.einsum(
        "srgpt,trge->srgpe", new_weights, fresh[:, :, :, 1], preferred_element_type=jnp.float32
    )
    attn = mixed.astype(jnp.bfloat16).reshape(steps, rows, local_groups * per_group * head_size)
    parts = lax.psum(1, "tp")
    blocks = attn.reshape(steps, parts, rows // parts, attn.shape[2])
    arrived = lax.all_to_all(blocks, "tp", split_axis=1, concat_axis=1, tiled=True)
    values = arrived.astype(jnp.float32)
    square_mean = jnp.mean(values * values, (1, 3), keepdims=True)
    gain = out_gain.astype(jnp.float32).reshape(1, parts, 1, attn.shape[2])
    normed = (values * lax.rsqrt(square_mean + 1e-05) * gain).astype(jnp.bfloat16)
    return normed.transpose(0, 2, 1, 3).reshape(steps, rows // parts, parts * attn.shape[2])


def solution(mesh):
    torus = Mesh(mesh.devices.reshape(8, 4, 2, 2, mesh.shape["tp"]), ("dp_0a", "dp_0b", "dp_1", "dp_2", "tp"))
    return jax.shard_map(
        per_device,
        mesh=torus,
        in_specs=(
            P(None, DP, None),
            P(DP_TP, None),
            P(None, DP, "tp"),
            P(DP, "tp", None, None, None),
            P(DP),
            P(),
        ),
        out_specs=P(None, DP_TP, None),
        check_vma=False,
    )
```
